128 devices in a mesh: col: 8 (over z, core), grp: 16 (over x, y).
Axes of the slice: x: 4, y: 4, z: 4, core: 2. Of those that a mesh axis runs over, the one named last changes fastest.
Arguments:
- factor_rows: float32 [1024, 4, 8, 512], P('grp', None, 'col'), may hold values from -3 to 3, as said below
- new_rows: float32 [8192, 4, 8, 512], P('grp', None, 'col'), may hold values from -0.3125 to 0.3125
Outputs:
- updated_rows: float32 [1024, 4, 8, 512], P('grp', None, 'col')
The draws below stay inside these ranges and needn't reach their ends.
Inputs may be any that keep to these rules, and one draw needn't show every extreme that they name: factor_rows is upper triangular in the global row and column numbers, with diagonal entries between 1 and 3.
All inputs are finite; a program needn't handle non-finite values.
Results may differ from the reference program's by a relative error of at most 0.00008.
Values sent between devices are 32-bit elements; how exact they have to be, the bound alone decides.
No kernel may reach another device: no remote copies, remote signals or barrier semaphores. Data moves between devices by JAX's collectives and lax.ppermute only.
A program may use at most 128 MiB of HBM per device.

```python
import jax
import jax.numpy as jnp
from jax import lax

N = 16384
B = 512
ROWS_GRP = 512
NPAN = 4
M = 8192
N_COL = 8
N_GRP = 16


def draw_factor_rows(key, part):
    spread = N // (NPAN * B)
    shape = (2 * B, NPAN, spread, B)
    key_off, key_diag = jax.random.split(jax.random.fold_in(key, 11))
    row_index = jax.lax.broadcasted_iota(jnp.int32, shape, 0)
    column = (jax.lax.broadcasted_iota(jnp.int32, shape, 1) * spread + jax.lax.broadcasted_iota(jnp.int32, shape, 2)) * B + jax.lax.broadcasted_iota(jnp.int32, shape, 3)
    above = jax.random.normal(key_off, shape, jnp.float32)
    above = above * (2.0 * B) ** (-0.5)
    diagonal = jax.random.uniform(key_diag, shape, jnp.float32, 1.0, 3.0)
    return jnp.where(column > row_index, above, jnp.where(column == row_index, diagonal, 0.0)).astype(jnp.float32)


def levels(rng, extent, pieces, least, high):
    gain, own = 1.0, jax.random.fold_in(rng, 6)
    for axis_at, shards_of in pieces:
        heights = jnp.exp(jax.random.uniform(jax.random.fold_in(own, axis_at), (shards_of,), jnp.float32, least / len(pieces), high / len(pieces)))
        gain = gain * jnp.repeat(heights, extent[axis_at] // shards_of).reshape([-1 if axis == axis_at else 1 for axis in range(len(extent))])
    return gain


def noise(key, extent, scale, reach, shards=(), dtype=jnp.bfloat16):
    values = scale * jax.random.normal(key, extent, jnp.float32)
    if shards:
        values = values * levels(key, extent, shards, -0.22, 0.18)
    return jnp.clip(values, -reach, reach).astype(dtype)


def setup_inputs(seed: int = 0) -> dict:
    arg_keys = jax.random.split(jax.random.key(seed), 3)
    return {
        "factor_rows": draw_factor_rows(jax.random.fold_in(arg_keys[2], 71), 0),
        "new_rows": noise(arg_keys[1], (M, NPAN, N_COL, B), (2.0 / (ROWS_GRP * N_GRP) ** 0.5), 0.3125, ((0, 16), (2, 8)), jnp.float32),
    }


def solve_lower(lower, right):
    return lax.linalg.triangular_solve(lower, right, left_side=True, lower=True)

def reference(factor_rows, new_rows):
    highest = lax.Precision.HIGHEST
    top = factor_rows.reshape(2 * B, N).astype(jnp.float32)
    data = new_rows.reshape(M, N).astype(jnp.float32)
    stacked = jnp.concatenate([top, data], 0)
    first = stacked[:, :B]
    second = stacked[:, B:2 * B]
    gram_one = jnp.dot(first.T, stacked, precision=highest)
    gram_two = jnp.dot(second.T, stacked, precision=highest)
    lower_one = jnp.linalg.cholesky(gram_one[:, :B])
    upper_one = solve_lower(lower_one, gram_one)
    cross = upper_one[:, B:2 * B]
    lower_two = jnp.linalg.cholesky(gram_two[:, B:2 * B] - jnp.dot(cross.T, cross, precision=highest))
    upper_two = solve_lower(lower_two, gram_two - jnp.dot(cross.T, upper_one, precision=highest))
    result = jnp.concatenate([upper_one, upper_two], 0)
    return result.reshape(2 * B, NPAN, N // (NPAN * B), B)
```

```python
import jax
import jax.numpy as jnp
from jax import lax
from jax.sharding import PartitionSpec as P


HIGHEST = lax.Precision.HIGHEST


def mm_t(a, b):
    return lax.dot_general(a, b, (((0,), (0,)), ((), ())), precision=HIGHEST,
                           preferred_element_type=jnp.float32)


def shards(factor_rows, new_rows):
    own_rows = factor_rows.shape[0]
    npanel = factor_rows.shape[1]
    width = factor_rows.shape[3]
    top = factor_rows.reshape(own_rows, npanel * width)
    data = new_rows.reshape(new_rows.shape[0], npanel * width)
    col = lax.axis_index("col")
    grp = lax.axis_index("grp")

    def spread(x):
        p = x[:, :width]
        z = jnp.zeros_like(p)
        return jnp.concatenate([jnp.where(col == 0, p, z), jnp.where(col == 1, p, z)], 1)

    both_top, both_data = lax.psum((spread(top), spread(data)), "col")
    first_top, second_top = both_top[:, :width], both_top[:, width:]
    first_data, second_data = both_data[:, :width], both_data[:, width:]

    g11 = mm_t(first_top, first_top) + mm_t(first_data, first_data)
    g2x = mm_t(second_top, both_top) + mm_t(second_data, both_data)
    g11, g2x = lax.psum((g11, g2x), "grp")

    gram = mm_t(both_top, top) + mm_t(both_data, data)
    gram, g11, g2x = lax.optimization_barrier((gram, g11, g2x))
    gram = lax.psum(gram, "grp")

    lower = jnp.concatenate(
        [jnp.concatenate([g11, jnp.zeros_like(g11)], 1), g2x], 0)
    chol = lax.linalg.cholesky(lower, symmetrize_input=False)
    n = 2 * width
    rows = lax.broadcasted_iota(jnp.int32, (own_rows, n), 0) + grp * own_rows
    cols = lax.broadcasted_iota(jnp.int32, (own_rows, n), 1)
    pick = (rows == cols).astype(jnp.float32)
    inv_rows = lax.linalg.triangular_solve(chol, pick, left_side=False, lower=True)
    mine = jnp.dot(inv_rows, gram, precision=HIGHEST, preferred_element_type=jnp.float32)
    return mine.reshape(own_rows, npanel, 1, width)


def solution(mesh):
    placed = (P("grp", None, "col", None), P("grp", None, "col", None))
    return jax.shard_map(
        shards, mesh=mesh, in_specs=placed, out_specs=P("grp", None, "col", None), check_vma=False
    )
```

```python
import jax
import jax.numpy as jnp
from jax import lax
from jax.sharding import PartitionSpec as P


HIGHEST = lax.Precision.HIGHEST


def mm_t(a, b):
    return lax.dot_general(a, b, (((0,), (0,)), ((), ())), precision=HIGHEST,
                           preferred_element_type=jnp.float32)


def shards(factor_rows, new_rows):
    own_rows = factor_rows.shape[0]
    npanel = factor_rows.shape[1]
    width = factor_rows.shape[3]
    top = factor_rows.reshape(own_rows, npanel * width)
    data = new_rows.reshape(new_rows.shape[0], npanel * width)
    col = lax.axis_index("col")
    grp = lax.axis_index("grp")

    def spread(x):
        p = x[:, :width]
        z = jnp.zeros_like(p)
        return jnp.concatenate([jnp.where(col == 0, p, z), jnp.where(col == 1, p, z)], 1)

    both_top, both_data = lax.psum((spread(top), spread(data)), "col")
    first_top, second_top = both_top[:, :width], both_top[:, width:]
    first_data, second_data = both_data[:, :width], both_data[:, width:]

    g11 = mm_t(first_top, first_top) + mm_t(first_data, first_data)
    g2x = mm_t(second_top, both_top) + mm_t(second_data, both_data)
    g11, g2x = lax.psum((g11, g2x), "grp")

    gram = mm_t(both_top, top) + mm_t(both_data, data)
    gram, g11, g2x = lax.optimization_barrier((gram, g11, g2x))
    gram = lax.psum(gram, "grp")

    lower = jnp.concatenate(
        [jnp.concatenate([g11, jnp.zeros_like(g11)], 1), g2x], 0)
    chol = lax.linalg.cholesky(lower, symmetrize_input=False)
    n = 2 * width
    blk = 128
    nb = n // blk
    chol4 = chol.reshape(nb, blk, nb, blk)
    diag = jnp.stack([chol4[k, :, k, :] for k in range(nb)])
    eye = jnp.broadcast_to(jnp.eye(blk, dtype=jnp.float32), (nb, blk, blk))
    dinv = lax.linalg.triangular_solve(diag, eye, left_side=True, lower=True)
    scaled = jnp.einsum("kab,kbn->kan", dinv, chol.reshape(nb, blk, n), precision=HIGHEST,
                        preferred_element_type=jnp.float32).reshape(n, n)
    bi = lax.broadcasted_iota(jnp.int32, (n, n), 0) // blk
    bj = lax.broadcasted_iota(jnp.int32, (n, n), 1) // blk
    strict = jnp.where(bi > bj, scaled, 0.0)
    rows = lax.broadcasted_iota(jnp.int32, (own_rows, n), 0) + grp * own_rows
    cols = lax.broadcasted_iota(jnp.int32, (own_rows, n), 1)
    pick = (rows == cols).astype(jnp.float32)
    acc = pick
    for _ in range(nb - 1):
        acc = pick - jnp.dot(acc, strict, precision=HIGHEST, preferred_element_type=jnp.float32)
    inv_rows = jnp.einsum("rkb,kbc->rkc", acc.reshape(own_rows, nb, blk), dinv, precision=HIGHEST,
                          preferred_element_type=jnp.float32).reshape(own_rows, n)
    mine = jnp.dot(inv_rows, gram, precision=HIGHEST, preferred_element_type=jnp.float32)
    return mine.reshape(own_rows, npanel, 1, width)


def solution(mesh):
    placed = (P("grp", None, "col", None), P("grp", None, "col", None))
    return jax.shard_map(
        shards, mesh=mesh, in_specs=placed, out_specs=P("grp", None, "col", None), check_vma=False
    )
```

```python
import jax
import jax.numpy as jnp
from jax import lax
from jax.sharding import PartitionSpec as P


HIGHEST = lax.Precision.HIGHEST


def mm_t(a, b):
    return lax.dot_general(a, b, (((0,), (0,)), ((), ())), precision=HIGHEST,
                           preferred_element_type=jnp.float32)


def tri_inverse(low):
    size = low.shape[-1]
    d = jnp.diagonal(low, axis1=1, axis2=2)
    eye = jnp.eye(size, dtype=jnp.float32)
    keep = jnp.tril(jnp.ones((size, size), jnp.bool_), -1)
    neg = jnp.where(keep, -(low / d[:, :, None]), 0.0)
    prod = eye + neg
    power = neg
    step = 2
    while step < size:
        power = jnp.einsum("kab,kbc->kac", power, power, precision=HIGHEST,
                           preferred_element_type=jnp.float32)
        prod = prod + jnp.einsum("kab,kbc->kac", prod, power, precision=HIGHEST,
                                 preferred_element_type=jnp.float32)
        step *= 2
    return prod / d[:, None, :]


def shards(factor_rows, new_rows):
    own_rows = factor_rows.shape[0]
    npanel = factor_rows.shape[1]
    width = factor_rows.shape[3]
    top = factor_rows.reshape(own_rows, npanel * width)
    data = new_rows.reshape(new_rows.shape[0], npanel * width)
    col = lax.axis_index("col")
    grp = lax.axis_index("grp")

    def spread(x):
        p = x[:, :width]
        z = jnp.zeros_like(p)
        return jnp.concatenate([jnp.where(col == 0, p, z), jnp.where(col == 1, p, z)], 1)

    both_top, both_data = lax.psum((spread(top), spread(data)), "col")
    first_top, second_top = both_top[:, :width], both_top[:, width:]
    first_data, second_data = both_data[:, :width], both_data[:, width:]

    g11 = mm_t(first_top, first_top) + mm_t(first_data, first_data)
    g2x = mm_t(second_top, both_top) + mm_t(second_data, both_data)
    g11, g2x = lax.psum((g11, g2x), "grp")

    gram = mm_t(both_top, top) + mm_t(both_data, data)
    gram, g11, g2x = lax.optimization_barrier((gram, g11, g2x))
    gram = lax.psum(gram, "grp")

    lower = jnp.concatenate(
        [jnp.concatenate([g11, jnp.zeros_like(g11)], 1), g2x], 0)
    chol = lax.linalg.cholesky(lower, symmetrize_input=False)
    n = 2 * width
    blk = 128
    nb = n // blk
    chol4 = chol.reshape(nb, blk, nb, blk)
    diag = jnp.stack([chol4[k, :, k, :] for k in range(nb)])
    dinv = tri_inverse(diag)
    scaled = jnp.einsum("kab,kbn->kan", dinv, chol.reshape(nb, blk, n), precision=HIGHEST,
                        preferred_element_type=jnp.float32).reshape(n, n)
    bi = lax.broadcasted_iota(jnp.int32, (n, n), 0) // blk
    bj = lax.broadcasted_iota(jnp.int32, (n, n), 1) // blk
    strict = jnp.where(bi > bj, scaled, 0.0)
    rows = lax.broadcasted_iota(jnp.int32, (own_rows, n), 0) + grp * own_rows
    cols = lax.broadcasted_iota(jnp.int32, (own_rows, n), 1)
    pick = (rows == cols).astype(jnp.float32)
    acc = pick
    for _ in range(nb - 1):
        acc = pick - jnp.dot(acc, strict, precision=HIGHEST, preferred_element_type=jnp.float32)
    inv_rows = jnp.einsum("rkb,kbc->rkc", acc.reshape(own_rows, nb, blk), dinv, precision=HIGHEST,
                          preferred_element_type=jnp.float32).reshape(own_rows, n)
    mine = jnp.dot(inv_rows, gram, precision=HIGHEST, preferred_element_type=jnp.float32)
    return mine.reshape(own_rows, npanel, 1, width)


def solution(mesh):
    placed = (P("grp", None, "col", None), P("grp", None, "col", None))
    return jax.shard_map(
        shards, mesh=mesh, in_specs=placed, out_specs=P("grp", None, "col", None), check_vma=False
    )
```

```python
import jax
import jax.numpy as jnp
from jax import lax
from jax.experimental import pallas as pl
from jax.sharding import PartitionSpec as P


HIGHEST = lax.Precision.HIGHEST


def mm_t(a, b):
    return lax.dot_general(a, b, (((0,), (0,)), ((), ())), precision=HIGHEST,
                           preferred_element_type=jnp.float32)


def tri_inverse(low):
    size = low.shape[-1]
    d = jnp.diagonal(low, axis1=1, axis2=2)
    eye = jnp.eye(size, dtype=jnp.float32)
    keep = jnp.tril(jnp.ones((size, size), jnp.bool_), -1)
    neg = jnp.where(keep, -(low / d[:, :, None]), 0.0)
    prod = eye + neg
    power = neg
    step = 2
    while step < size:
        power = jnp.einsum("kab,kbc->kac", power, power, precision=HIGHEST,
                           preferred_element_type=jnp.float32)
        prod = prod + jnp.einsum("kab,kbc->kac", prod, power, precision=HIGHEST,
                                 preferred_element_type=jnp.float32)
        step *= 2
    return prod / d[:, None, :]


def chol_inv_kernel(a_ref, w_ref):
    n = a_ref.shape[0]
    a = a_ref[...]
    row_id = lax.broadcasted_iota(jnp.int32, (n, n), 0)
    col_id = lax.broadcasted_iota(jnp.int32, (n, n), 1)
    w = (row_id == col_id).astype(jnp.float32)

    def body(j, carry):
        a, w = carry
        rsel = row_id == j
        arow = jnp.sum(jnp.where(rsel, a, 0.0), axis=0, keepdims=True)
        acol = jnp.sum(jnp.where(col_id == j, a, 0.0), axis=1, keepdims=True)
        piv = jnp.sum(jnp.where(col_id[0:1, :] == j, arow, 0.0), axis=1, keepdims=True)
        r = lax.rsqrt(piv)
        lrow = arow * r
        lcol = acol * r
        a = a - lcol * lrow
        wrow = jnp.sum(jnp.where(rsel, w, 0.0), axis=0, keepdims=True) * r
        below = jnp.where(row_id[:, 0:1] > j, lcol, 0.0)
        w = jnp.where(rsel, wrow, w - below * wrow)
        return a, w

    a, w = lax.fori_loop(0, n, body, (a, w))
    w_ref[...] = w


def chol_inv(a):
    return pl.pallas_call(chol_inv_kernel, out_shape=jax.ShapeDtypeStruct(a.shape, jnp.float32))(a)


def mm_nt(a, b):
    return lax.dot_general(a, b, (((1,), (1,)), ((), ())), precision=HIGHEST,
                           preferred_element_type=jnp.float32)


def block_chol_inv(full, blk):
    n = full.shape[0]
    nb = n // blk
    t = full
    ws, cols = [], []
    for k in range(nb):
        w = chol_inv(t[:blk, :blk])
        ws.append(w)
        if k < nb - 1:
            panel = mm_nt(t[blk:, :blk], w)
            cols.append(jnp.concatenate([jnp.zeros(((k + 1) * blk, blk), jnp.float32), panel], 0))
            t = t[blk:, blk:] - mm_nt(panel, panel)
        else:
            cols.append(jnp.zeros((n, blk), jnp.float32))
    return jnp.stack(ws), jnp.concatenate(cols, 1)


def shards(factor_rows, new_rows):
    own_rows = factor_rows.shape[0]
    npanel = factor_rows.shape[1]
    width = factor_rows.shape[3]
    top = factor_rows.reshape(own_rows, npanel * width)
    data = new_rows.reshape(new_rows.shape[0], npanel * width)
    col = lax.axis_index("col")
    grp = lax.axis_index("grp")

    def spread(x):
        p = x[:, 0, 0, :]
        z = jnp.zeros_like(p)
        return jnp.concatenate([jnp.where(col == 0, p, z), jnp.where(col == 1, p, z)], 1)

    both_top, both_data = lax.psum((spread(factor_rows), spread(new_rows)), "col")
    first_top, second_top = both_top[:, :width], both_top[:, width:]
    first_data, second_data = both_data[:, :width], both_data[:, width:]

    g11 = mm_t(first_top, first_top) + mm_t(first_data, first_data)
    g2x = mm_t(second_top, both_top) + mm_t(second_data, both_data)
    g11, g2x = lax.psum((g11, g2x), "grp")

    gram = mm_t(both_top, top) + mm_t(both_data, data)
    gram, g11, g2x = lax.optimization_barrier((gram, g11, g2x))
    gram = lax.psum(gram, "grp")

    lower = jnp.concatenate(
        [jnp.concatenate([g11, jnp.zeros_like(g11)], 1), g2x], 0)
    n = 2 * width
    blk = 128
    nb = n // blk
    ii = lax.broadcasted_iota(jnp.int32, (n, n), 0)
    jj = lax.broadcasted_iota(jnp.int32, (n, n), 1)
    full = jnp.where(ii >= jj, lower, lower.T)
    dinv, strict_low = block_chol_inv(full, blk)
    strict = jnp.einsum("kab,kbn->kan", dinv, strict_low.reshape(nb, blk, n), precision=HIGHEST,
                        preferred_element_type=jnp.float32).reshape(n, n)
    rows = lax.broadcasted_iota(jnp.int32, (own_rows, n), 0) + grp * own_rows
    cols = lax.broadcasted_iota(jnp.int32, (own_rows, n), 1)
    pick = (rows == cols).astype(jnp.float32)
    acc = pick
    for _ in range(nb - 1):
        acc = pick - jnp.dot(acc, strict, precision=HIGHEST, preferred_element_type=jnp.float32)
    inv_rows = jnp.einsum("rkb,kbc->rkc", acc.reshape(own_rows, nb, blk), dinv, precision=HIGHEST,
                          preferred_element_type=jnp.float32).reshape(own_rows, n)
    mine = jnp.dot(inv_rows, gram, precision=HIGHEST, preferred_element_type=jnp.float32)
    return mine.reshape(own_rows, npanel, 1, width)


def solution(mesh):
    placed = (P("grp", None, "col", None), P("grp", None, "col", None))
    return jax.shard_map(
        shards, mesh=mesh, in_specs=placed, out_specs=P("grp", None, "col", None), check_vma=False
    )
```

```python
import jax
import jax.numpy as jnp
from jax import lax
from jax.experimental import pallas as pl
from jax.sharding import PartitionSpec as P


HIGHEST = lax.Precision.HIGHEST


def mm_t(a, b):
    return lax.dot_general(a, b, (((0,), (0,)), ((), ())), precision=HIGHEST,
                           preferred_element_type=jnp.float32)


def tri_inverse(low):
    size = low.shape[-1]
    d = jnp.diagonal(low, axis1=1, axis2=2)
    eye = jnp.eye(size, dtype=jnp.float32)
    keep = jnp.tril(jnp.ones((size, size), jnp.bool_), -1)
    neg = jnp.where(keep, -(low / d[:, :, None]), 0.0)
    prod = eye + neg
    power = neg
    step = 2
    while step < size:
        power = jnp.einsum("kab,kbc->kac", power, power, precision=HIGHEST,
                           preferred_element_type=jnp.float32)
        prod = prod + jnp.einsum("kab,kbc->kac", prod, power, precision=HIGHEST,
                                 preferred_element_type=jnp.float32)
        step *= 2
    return prod / d[:, None, :]


def chol_inv_kernel(a_ref, w_ref):
    n = a_ref.shape[0]
    a = a_ref[...]
    row_id = lax.broadcasted_iota(jnp.int32, (n, n), 0)
    col_id = lax.broadcasted_iota(jnp.int32, (n, n), 1)
    w = (row_id == col_id).astype(jnp.float32)

    def body(j, carry):
        a, w = carry
        rsel = row_id == j
        arow = jnp.sum(jnp.where(rsel, a, 0.0), axis=0, keepdims=True)
        acol = jnp.sum(jnp.where(col_id == j, a, 0.0), axis=1, keepdims=True)
        piv = jnp.sum(jnp.where(col_id[0:1, :] == j, arow, 0.0), axis=1, keepdims=True)
        r = lax.rsqrt(piv)
        lrow = arow * r
        lcol = acol * r
        a = a - lcol * lrow
        wrow = jnp.sum(jnp.where(rsel, w, 0.0), axis=0, keepdims=True) * r
        below = jnp.where(row_id[:, 0:1] > j, lcol, 0.0)
        w = jnp.where(rsel, wrow, w - below * wrow)
        return a, w

    a, w = lax.fori_loop(0, n, body, (a, w))
    w_ref[...] = w


def chol_inv(a):
    return pl.pallas_call(chol_inv_kernel, out_shape=jax.ShapeDtypeStruct(a.shape, jnp.float32))(a)


def mm_nt(a, b):
    return lax.dot_general(a, b, (((1,), (1,)), ((), ())), precision=HIGHEST,
                           preferred_element_type=jnp.float32)


def block_chol_inv(full, blk):
    n = full.shape[0]
    nb = n // blk
    t = full
    ws, cols = [], []
    for k in range(nb):
        w = chol_inv(t[:blk, :blk])
        ws.append(w)
        if k < nb - 1:
            panel = mm_nt(t[blk:, :blk], w)
            cols.append(jnp.concatenate([jnp.zeros(((k + 1) * blk, blk), jnp.float32), panel], 0))
            t = t[blk:, blk:] - mm_nt(panel, panel)
        else:
            cols.append(jnp.zeros((n, blk), jnp.float32))
    return jnp.stack(ws), jnp.concatenate(cols, 1)


def shards(factor_rows, new_rows):
    own_rows = factor_rows.shape[0]
    npanel = factor_rows.shape[1]
    width = factor_rows.shape[3]
    top = factor_rows.reshape(own_rows, npanel * width)
    data = new_rows.reshape(new_rows.shape[0], npanel * width)
    col = lax.axis_index("col")
    grp = lax.axis_index("grp")

    def spread(x):
        p = x[:, 0, 0, :]
        z = jnp.zeros_like(p)
        return jnp.concatenate([jnp.where(col == 0, p, z), jnp.where(col == 1, p, z)], 1)

    both_top, both_data = lax.psum((spread(factor_rows), spread(new_rows)), "col")
    first_top, second_top = both_top[:, :width], both_top[:, width:]
    first_data, second_data = both_data[:, :width], both_data[:, width:]

    g11 = mm_t(first_top, first_top) + mm_t(first_data, first_data)
    g2x = mm_t(second_top, both_top) + mm_t(second_data, both_data)
    g11, g2x = lax.psum((g11, g2x), "grp")

    gram = (mm_t(both_top, top) + mm_t(both_data, data)).T
    gram, g11, g2x = lax.optimization_barrier((gram, g11, g2x))
    gram = lax.psum(gram, "grp")

    n = 2 * width
    blk = 128
    nb = n // blk
    full = jnp.concatenate(
        [jnp.concatenate([g11, g2x[:, :width].T], 1), g2x], 0)
    dinv, strict_low = block_chol_inv(full, blk)
    strict = jnp.einsum("kab,kbn->kan", dinv, strict_low.reshape(nb, blk, n), precision=HIGHEST,
                        preferred_element_type=jnp.float32).reshape(n, n)
    rows = lax.broadcasted_iota(jnp.int32, (own_rows, n), 0) + grp * own_rows
    cols = lax.broadcasted_iota(jnp.int32, (own_rows, n), 1)
    pick = (rows == cols).astype(jnp.float32)
    acc = pick
    for _ in range(nb - 1):
        acc = pick - jnp.dot(acc, strict, precision=HIGHEST, preferred_element_type=jnp.float32)
    inv_rows = jnp.einsum("rkb,kbc->rkc", acc.reshape(own_rows, nb, blk), dinv, precision=HIGHEST,
                          preferred_element_type=jnp.float32).reshape(own_rows, n)
    mine = mm_nt(inv_rows, gram)
    return mine.reshape(own_rows, npanel, 1, width)


def solution(mesh):
    placed = (P("grp", None, "col", None), P("grp", None, "col", None))
    return jax.shard_map(
        shards, mesh=mesh, in_specs=placed, out_specs=P("grp", None, "col", None), check_vma=False
    )
```

```python
import jax
import jax.numpy as jnp
from jax import lax
from jax.experimental import pallas as pl
from jax.sharding import PartitionSpec as P


HIGHEST = lax.Precision.HIGHEST


def mm_t(a, b):
    return lax.dot_general(a, b, (((0,), (0,)), ((), ())), precision=HIGHEST,
                           preferred_element_type=jnp.float32)


def tri_inverse(low):
    size = low.shape[-1]
    d = jnp.diagonal(low, axis1=1, axis2=2)
    eye = jnp.eye(size, dtype=jnp.float32)
    keep = jnp.tril(jnp.ones((size, size), jnp.bool_), -1)
    neg = jnp.where(keep, -(low / d[:, :, None]), 0.0)
    prod = eye + neg
    power = neg
    step = 2
    while step < size:
        power = jnp.einsum("kab,kbc->kac", power, power, precision=HIGHEST,
                           preferred_element_type=jnp.float32)
        prod = prod + jnp.einsum("kab,kbc->kac", prod, power, precision=HIGHEST,
                                 preferred_element_type=jnp.float32)
        step *= 2
    return prod / d[:, None, :]


def chol_inv_kernel(a_ref, w_ref):
    n = a_ref.shape[0]
    a = a_ref[...]
    row_id = lax.broadcasted_iota(jnp.int32, (n, n), 0)
    col_id = lax.broadcasted_iota(jnp.int32, (n, n), 1)
    w = (row_id == col_id).astype(jnp.float32)

    def body(j, carry):
        a, w = carry
        rsel = row_id == j
        arow = jnp.sum(jnp.where(rsel, a, 0.0), axis=0, keepdims=True)
        acol = jnp.sum(jnp.where(col_id == j, a, 0.0), axis=1, keepdims=True)
        piv = jnp.sum(jnp.where(col_id[0:1, :] == j, arow, 0.0), axis=1, keepdims=True)
        r = lax.rsqrt(piv)
        lrow = arow * r
        lcol = acol * r
        a = a - lcol * lrow
        wrow = jnp.sum(jnp.where(rsel, w, 0.0), axis=0, keepdims=True) * r
        below = jnp.where(row_id[:, 0:1] > j, lcol, 0.0)
        w = jnp.where(rsel, wrow, w - below * wrow)
        return a, w

    a, w = lax.fori_loop(0, n, body, (a, w))
    w_ref[...] = w


def chol_inv(a):
    return pl.pallas_call(chol_inv_kernel, out_shape=jax.ShapeDtypeStruct(a.shape, jnp.float32))(a)


def mm_nt(a, b):
    return lax.dot_general(a, b, (((1,), (1,)), ((), ())), precision=HIGHEST,
                           preferred_element_type=jnp.float32)


def block_chol_inv(full, blk):
    n = full.shape[0]
    nb = n // blk
    t = full
    rhs = jnp.eye(n, dtype=jnp.float32)
    ys = []
    for k in range(nb):
        w = chol_inv(t[:blk, :blk])
        y = jnp.dot(w, rhs[:blk], precision=HIGHEST, preferred_element_type=jnp.float32)
        ys.append(y)
        if k < nb - 1:
            panel = mm_nt(t[blk:, :blk], w)
            t = t[blk:, blk:] - mm_nt(panel, panel)
            rhs = rhs[blk:] - jnp.dot(panel, y, precision=HIGHEST, preferred_element_type=jnp.float32)
    return jnp.concatenate(ys, 0)


def shards(factor_rows, new_rows):
    own_rows = factor_rows.shape[0]
    npanel = factor_rows.shape[1]
    width = factor_rows.shape[3]
    top = factor_rows.reshape(own_rows, npanel * width)
    data = new_rows.reshape(new_rows.shape[0], npanel * width)
    col = lax.axis_index("col")
    grp = lax.axis_index("grp")

    def spread(x):
        p = x[:, 0, 0, :]
        z = jnp.zeros_like(p)
        return jnp.concatenate([jnp.where(col == 0, p, z), jnp.where(col == 1, p, z)], 1)

    both_top, both_data = lax.psum((spread(factor_rows), spread(new_rows)), "col")
    first_top, second_top = both_top[:, :width], both_top[:, width:]
    first_data, second_data = both_data[:, :width], both_data[:, width:]

    g11 = mm_t(first_top, first_top) + mm_t(first_data, first_data)
    g2x = mm_t(second_top, both_top) + mm_t(second_data, both_data)
    g11, g2x = lax.psum((g11, g2x), "grp")

    gram = (mm_t(both_top, top) + mm_t(both_data, data)).T
    gram, g11, g2x = lax.optimization_barrier((gram, g11, g2x))
    gram = lax.psum(gram, "grp")

    n = 2 * width
    blk = 128
    nb = n // blk
    full = jnp.concatenate(
        [jnp.concatenate([g11, g2x[:, :width].T], 1), g2x], 0)
    inverse = block_chol_inv(full, blk)
    inv_rows = lax.dynamic_slice_in_dim(inverse, grp * own_rows, own_rows, 0)
    mine = mm_nt(inv_rows, gram)
    return mine.reshape(own_rows, npanel, 1, width)


def solution(mesh):
    placed = (P("grp", None, "col", None), P("grp", None, "col", None))
    return jax.shard_map(
        shards, mesh=mesh, in_specs=placed, out_specs=P("grp", None, "col", None), check_vma=False
    )
```

```python
import jax
import jax.numpy as jnp
from jax import lax
from jax.experimental import pallas as pl
from jax.sharding import PartitionSpec as P


HIGHEST = lax.Precision.HIGHEST


def mm_t(a, b):
    return lax.dot_general(a, b, (((0,), (0,)), ((), ())), precision=HIGHEST,
                           preferred_element_type=jnp.float32)


def chol_inv_kernel(a_ref, w_ref):
    n = a_ref.shape[0]
    a = a_ref[...]
    full_row = lax.broadcasted_iota(jnp.int32, (n, n), 0)
    full_col = lax.broadcasted_iota(jnp.int32, (n, n), 1)
    w = (full_row == full_col).astype(jnp.float32)
    for t in range(n // 8):
        m = n - 8 * t
        row_id = lax.broadcasted_iota(jnp.int32, (m, n), 0) + 8 * t
        col_id = lax.broadcasted_iota(jnp.int32, (m, n), 1)

        def body(j, carry, row_id=row_id, col_id=col_id):
            a, w = carry
            rsel = row_id == j
            arow = jnp.sum(jnp.where(rsel, a, 0.0), axis=0, keepdims=True)
            acol = jnp.sum(jnp.where(col_id == j, a, 0.0), axis=1, keepdims=True)
            piv = jnp.sum(jnp.where(col_id[0:1, :] == j, arow, 0.0), axis=1, keepdims=True)
            r = lax.rsqrt(piv)
            lrow = arow * r
            lcol = acol * r
            a = a - lcol * lrow
            wrow = jnp.sum(jnp.where(rsel, w, 0.0), axis=0, keepdims=True) * r
            below = jnp.where(row_id[:, 0:1] > j, lcol, 0.0)
            w = jnp.where(rsel, wrow, w - below * wrow)
            return a, w

        a, w = lax.fori_loop(8 * t, 8 * t + 8, body, (a, w))
        w_ref[8 * t:8 * t + 8, :] = w[:8]
        a = a[8:]
        w = w[8:]


def chol_inv(a):
    return pl.pallas_call(chol_inv_kernel, out_shape=jax.ShapeDtypeStruct(a.shape, jnp.float32))(a)


def mm_nt(a, b):
    return lax.dot_general(a, b, (((1,), (1,)), ((), ())), precision=HIGHEST,
                           preferred_element_type=jnp.float32)


def block_chol_inv(full, blk):
    n = full.shape[0]
    nb = n // blk
    t = full
    rhs = jnp.eye(n, dtype=jnp.float32)
    ys = []
    for k in range(nb):
        w = chol_inv(t[:blk, :blk])
        y = jnp.dot(w, rhs[:blk], precision=HIGHEST, preferred_element_type=jnp.float32)
        ys.append(y)
        if k < nb - 1:
            panel = mm_nt(t[blk:, :blk], w)
            t = t[blk:, blk:] - mm_nt(panel, panel)
            rhs = rhs[blk:] - jnp.dot(panel, y, precision=HIGHEST, preferred_element_type=jnp.float32)
    return jnp.concatenate(ys, 0)


def shards(factor_rows, new_rows):
    own_rows = factor_rows.shape[0]
    npanel = factor_rows.shape[1]
    width = factor_rows.shape[3]
    top = factor_rows.reshape(own_rows, npanel * width)
    data = new_rows.reshape(new_rows.shape[0], npanel * width)
    col = lax.axis_index("col")
    grp = lax.axis_index("grp")

    def spread(x):
        p = x[:, 0, 0, :]
        z = jnp.zeros_like(p)
        return jnp.concatenate([jnp.where(col == 0, p, z), jnp.where(col == 1, p, z)], 1)

    both_top, both_data = lax.psum((spread(factor_rows), spread(new_rows)), "col")
    first_top, second_top = both_top[:, :width], both_top[:, width:]
    first_data, second_data = both_data[:, :width], both_data[:, width:]

    g11 = mm_t(first_top, first_top) + mm_t(first_data, first_data)
    g2x = mm_t(second_top, both_top) + mm_t(second_data, both_data)
    g11, g2x = lax.psum((g11, g2x), "grp")

    gram = (mm_t(both_top, top) + mm_t(both_data, data)).T
    gram, g11, g2x = lax.optimization_barrier((gram, g11, g2x))
    gram = lax.psum(gram, "grp")

    n = 2 * width
    blk = 128
    nb = n // blk
    full = jnp.concatenate(
        [jnp.concatenate([g11, g2x[:, :width].T], 1), g2x], 0)
    inverse = block_chol_inv(full, blk)
    inv_rows = lax.dynamic_slice_in_dim(inverse, grp * own_rows, own_rows, 0)
    mine = mm_nt(inv_rows, gram)
    return mine.reshape(own_rows, npanel, 1, width)


def solution(mesh):
    placed = (P("grp", None, "col", None), P("grp", None, "col", None))
    return jax.shard_map(
        shards, mesh=mesh, in_specs=placed, out_specs=P("grp", None, "col", None), check_vma=False
    )
```

```python
import jax
import jax.numpy as jnp
from jax import lax
from jax.experimental import pallas as pl
from jax.sharding import PartitionSpec as P


HIGHEST = lax.Precision.HIGHEST


def mm_t(a, b):
    return lax.dot_general(a, b, (((0,), (0,)), ((), ())), precision=HIGHEST,
                           preferred_element_type=jnp.float32)


def chol_inv_kernel(a_ref, w_ref):
    n = a_ref.shape[0]
    a = a_ref[...]
    full_row = lax.broadcasted_iota(jnp.int32, (n, n), 0)
    full_col = lax.broadcasted_iota(jnp.int32, (n, n), 1)
    w = (full_row == full_col).astype(jnp.float32)
    for t in range(n // 8):
        m = n - 8 * t
        row_id = lax.broadcasted_iota(jnp.int32, (m, n), 0) + 8 * t
        col_id = lax.broadcasted_iota(jnp.int32, (m, n), 1)

        def body(j, carry, row_id=row_id, col_id=col_id):
            a, w = carry
            rsel = row_id == j
            arow = jnp.sum(jnp.where(rsel, a, 0.0), axis=0, keepdims=True)
            acol = jnp.sum(jnp.where(col_id == j, a, 0.0), axis=1, keepdims=True)
            piv = jnp.sum(jnp.where(row_id[:, 0:1] == j, acol, 0.0), axis=0, keepdims=True)
            r = lax.rsqrt(piv)
            lrow = arow * r
            lcol = acol * r
            a = a - lcol * lrow
            wrow = jnp.sum(jnp.where(rsel, w, 0.0), axis=0, keepdims=True) * r
            below = jnp.where(row_id[:, 0:1] > j, lcol, 0.0)
            w = jnp.where(rsel, wrow, w - below * wrow)
            return a, w

        a, w = lax.fori_loop(8 * t, 8 * t + 8, body, (a, w), unroll=8)
        w_ref[8 * t:8 * t + 8, :] = w[:8]
        a = a[8:]
        w = w[8:]


def chol_inv(a):
    return pl.pallas_call(chol_inv_kernel, out_shape=jax.ShapeDtypeStruct(a.shape, jnp.float32))(a)


def mm_nt(a, b):
    return lax.dot_general(a, b, (((1,), (1,)), ((), ())), precision=HIGHEST,
                           preferred_element_type=jnp.float32)


def block_chol_inv(full, blk):
    n = full.shape[0]
    nb = n // blk
    t = full
    rhs = jnp.eye(n, dtype=jnp.float32)
    ys = []
    for k in range(nb):
        w = chol_inv(t[:blk, :blk])
        y = jnp.dot(w, rhs[:blk], precision=HIGHEST, preferred_element_type=jnp.float32)
        ys.append(y)
        if k < nb - 1:
            panel = mm_nt(t[blk:, :blk], w)
            t = t[blk:, blk:] - mm_nt(panel, panel)
            rhs = rhs[blk:] - jnp.dot(panel, y, precision=HIGHEST, preferred_element_type=jnp.float32)
    return jnp.concatenate(ys, 0)


def shards(factor_rows, new_rows):
    own_rows = factor_rows.shape[0]
    npanel = factor_rows.shape[1]
    width = factor_rows.shape[3]
    top = factor_rows.reshape(own_rows, npanel * width)
    data = new_rows.reshape(new_rows.shape[0], npanel * width)
    col = lax.axis_index("col")
    grp = lax.axis_index("grp")

    def spread(x):
        p = x[:, 0, 0, :]
        z = jnp.zeros_like(p)
        return jnp.concatenate([jnp.where(col == 0, p, z), jnp.where(col == 1, p, z)], 1)

    both_top, both_data = lax.psum((spread(factor_rows), spread(new_rows)), "col")
    first_top, second_top = both_top[:, :width], both_top[:, width:]
    first_data, second_data = both_data[:, :width], both_data[:, width:]

    g11 = mm_t(first_top, first_top) + mm_t(first_data, first_data)
    g2x = mm_t(second_top, both_top) + mm_t(second_data, both_data)
    g11, g2x = lax.psum((g11, g2x), "grp")

    gram = (mm_t(both_top, top) + mm_t(both_data, data)).T
    gram, g11, g2x = lax.optimization_barrier((gram, g11, g2x))
    gram = lax.psum(gram, "grp")

    n = 2 * width
    blk = 128
    nb = n // blk
    full = jnp.concatenate(
        [jnp.concatenate([g11, g2x[:, :width].T], 1), g2x], 0)
    inverse = block_chol_inv(full, blk)
    inv_rows = lax.dynamic_slice_in_dim(inverse, grp * own_rows, own_rows, 0)
    mine = mm_nt(inv_rows, gram)
    return mine.reshape(own_rows, npanel, 1, width)


def solution(mesh):
    placed = (P("grp", None, "col", None), P("grp", None, "col", None))
    return jax.shard_map(
        shards, mesh=mesh, in_specs=placed, out_specs=P("grp", None, "col", None), check_vma=False
    )
```

```python
import jax
import jax.numpy as jnp
from jax import lax
from jax.experimental import pallas as pl
from jax.sharding import PartitionSpec as P


HIGHEST = lax.Precision.HIGHEST


def mm_t(a, b):
    return lax.dot_general(a, b, (((0,), (0,)), ((), ())), precision=HIGHEST,
                           preferred_element_type=jnp.float32)


def chol_inv_kernel(a_ref, w_ref):
    n = a_ref.shape[0]
    a = a_ref[...]
    full_row = lax.broadcasted_iota(jnp.int32, (n, n), 0)
    full_col = lax.broadcasted_iota(jnp.int32, (n, n), 1)
    w = (full_row == full_col).astype(jnp.float32)
    for t in range(n // 8):
        m = n - 8 * t
        row_id = lax.broadcasted_iota(jnp.int32, (m, n), 0) + 8 * t
        col_id = lax.broadcasted_iota(jnp.int32, (m, n), 1)

        def body(j, carry, row_id=row_id, col_id=col_id):
            a, w = carry
            rsel = row_id == j
            arow = jnp.sum(jnp.where(rsel, a, 0.0), axis=0, keepdims=True)
            acol = jnp.sum(jnp.where(col_id == j, a, 0.0), axis=1, keepdims=True)
            piv = jnp.sum(jnp.where(row_id[:, 0:1] == j, acol, 0.0), axis=0, keepdims=True)
            r = lax.rsqrt(piv)
            lrow = arow * r
            lcol = acol * r
            a = a - lcol * lrow
            wrow = jnp.sum(jnp.where(rsel, w, 0.0), axis=0, keepdims=True) * r
            below = jnp.where(row_id[:, 0:1] > j, lcol, 0.0)
            w = jnp.where(rsel, wrow, w - below * wrow)
            return a, w

        a, w = lax.fori_loop(8 * t, 8 * t + 8, body, (a, w), unroll=8)
        w_ref[8 * t:8 * t + 8, :] = w[:8]
        a = a[8:]
        w = w[8:]


def chol_inv(a):
    return pl.pallas_call(chol_inv_kernel, out_shape=jax.ShapeDtypeStruct(a.shape, jnp.float32))(a)


def mm_nt(a, b):
    return lax.dot_general(a, b, (((1,), (1,)), ((), ())), precision=HIGHEST,
                           preferred_element_type=jnp.float32)


def block_chol_inv(full, blk):
    n = full.shape[0]
    nb = n // blk
    t = full
    eye = jnp.eye(n, dtype=jnp.float32)
    left = None
    ys = []
    for k in range(nb):
        lo, hi = k * blk, (k + 1) * blk
        cur = eye[lo:, lo:hi] if left is None else jnp.concatenate([left, eye[lo:, lo:hi]], 1)
        w = chol_inv(t[:blk, :blk])
        y = jnp.dot(w, cur[:blk], precision=HIGHEST, preferred_element_type=jnp.float32)
        ys.append(jnp.concatenate([y, jnp.zeros((blk, n - hi), jnp.float32)], 1))
        if k < nb - 1:
            panel = mm_nt(t[blk:, :blk], w)
            t = t[blk:, blk:] - mm_nt(panel, panel)
            left = cur[blk:] - jnp.dot(panel, y, precision=HIGHEST, preferred_element_type=jnp.float32)
    return jnp.concatenate(ys, 0)


def shards(factor_rows, new_rows):
    own_rows = factor_rows.shape[0]
    npanel = factor_rows.shape[1]
    width = factor_rows.shape[3]
    top = factor_rows.reshape(own_rows, npanel * width)
    data = new_rows.reshape(new_rows.shape[0], npanel * width)
    col = lax.axis_index("col")
    grp = lax.axis_index("grp")

    def spread(x):
        p = x[:, 0, 0, :]
        z = jnp.zeros_like(p)
        return jnp.concatenate([jnp.where(col == 0, p, z), jnp.where(col == 1, p, z)], 1)

    both_top, both_data = lax.psum((spread(factor_rows), spread(new_rows)), "col")
    first_top, second_top = both_top[:, :width], both_top[:, width:]
    first_data, second_data = both_data[:, :width], both_data[:, width:]

    g11 = mm_t(first_top, first_top) + mm_t(first_data, first_data)
    g2x = mm_t(second_top, both_top) + mm_t(second_data, both_data)
    g11, g2x = lax.psum((g11, g2x), "grp")

    gram = (mm_t(both_top, top) + mm_t(both_data, data)).T
    gram, g11, g2x = lax.optimization_barrier((gram, g11, g2x))
    gram = lax.psum(gram, "grp")

    n = 2 * width
    blk = 128
    nb = n // blk
    full = jnp.concatenate(
        [jnp.concatenate([g11, g2x[:, :width].T], 1), g2x], 0)
    inverse = block_chol_inv(full, blk)
    inv_rows = lax.dynamic_slice_in_dim(inverse, grp * own_rows, own_rows, 0)
    mine = mm_nt(inv_rows, gram)
    return mine.reshape(own_rows, npanel, 1, width)


def solution(mesh):
    placed = (P("grp", None, "col", None), P("grp", None, "col", None))
    return jax.shard_map(
        shards, mesh=mesh, in_specs=placed, out_specs=P("grp", None, "col", None), check_vma=False
    )
```
